512 devices in a mesh: node: 64 (over z, x), local: 8 (over y, core).
Axes of the slice: x: 4, y: 4, z: 16, core: 2. Of those that a mesh axis runs over, the one named last changes fastest.
Arguments:
- tokens: bfloat16 [8192, 4096], P('node', 'local'), may hold values from -6 to 6
- route_ids: int32 [8192, 4], P('node'), may hold values from 0 to 63, as said below
- route_slots: int32 [8192, 4], P('node'), may hold values from 0 to 9, as said below
- keep_mask: int32 [8192, 4], P('node'), may hold values from 0 to 1
- route_weights: float32 [8192, 4], P('node'), may hold values from 0.05 to 0.6
- gate_weight: bfloat16 [64, 4096, 1024], P('node', None, 'local'), may hold values from -0.09375 to 0.09375
- up_weight: bfloat16 [64, 4096, 1024], P('node', None, 'local'), may hold values from -0.09375 to 0.09375
- down_weight: bfloat16 [64, 1024, 4096], P('node', None, 'local'), may hold values from -0.1875 to 0.1875
Outputs:
- combined: bfloat16 [8192, 4096], P('node', 'local')
The draws below stay inside these ranges and needn't reach their ends.
Inputs may be any that keep to these rules, and one draw needn't show every extreme that they name: `route_ids`: each row names 4 different experts. `route_slots`: kept routes of the tokens of one node group to one expert have distinct slots; in every draw some expert has all 10 slots kept for every node group.
All inputs are finite; a program needn't handle non-finite values.
Results may differ from the reference program's by a relative error of at most 0.0057.
Values may be sent and summed in bfloat16 or wider, within the bound.
No kernel may reach another device: no remote copies, remote signals or barrier semaphores. Data moves between devices by JAX's collectives and lax.ppermute only.
A program may use at most 64 MiB of HBM per device.

```python
import jax
import jax.numpy as jnp
from jax import lax

D = 4096
HID = 1024
TOPK = 4
TOK_G = 128
EXPERT_TOTAL = 64
TOKENS = 8192
SLOT_LIMIT = 10


def route_table(key):
    starting_score = jax.random.randint(jax.random.fold_in(key, 11), (TOKENS, EXPERT_TOTAL), 0, 65536)
    expert_demand = jax.random.randint(jax.random.fold_in(key, 12), (EXPERT_TOTAL,), 0, 4) * 16384
    favored_expert = jax.random.randint(jax.random.fold_in(key, 13), (), 0, EXPERT_TOTAL)
    within_group = jnp.arange(TOKENS, dtype=jnp.int32) % TOK_G
    expert_number = jnp.arange(EXPERT_TOTAL, dtype=jnp.int32)
    extra_reward = jnp.where((within_group[:, None] < SLOT_LIMIT) & (expert_number[None, :] == favored_expert), 4194304, 0)
    router_score = (starting_score + expert_demand[None, :] + extra_reward) * EXPERT_TOTAL + expert_number[None, :]
    _, chosen = lax.top_k(router_score, TOPK)
    chosen = chosen.astype(jnp.int32)
    blocks = TOKENS // TOK_G
    onehot = (chosen.reshape(blocks, TOK_G * TOPK)[:, :, None] == expert_number[None, None, :]).astype(jnp.int32)
    earlier = jnp.cumsum(onehot, axis=1) - onehot
    rank = jnp.sum(earlier * onehot, axis=2).reshape(TOKENS, TOPK)
    return (chosen, rank.astype(jnp.int32))


def draw_route_ids(key, part):
    chosen, rank = route_table(key)
    return chosen


def draw_route_slots(key, part):
    chosen, rank = route_table(key)
    return jnp.minimum(rank, SLOT_LIMIT - 1).astype(jnp.int32)


def draw_keep_mask(key, part):
    chosen, rank = route_table(key)
    return (rank < SLOT_LIMIT).astype(jnp.int32)


def block_levels(rng, shape, cuts, smallest, largest):
    gain, own = 1.0, jax.random.fold_in(rng, 6)
    for dim, parts in cuts:
        draws = jnp.exp(jax.random.uniform(jax.random.fold_in(own, dim), (parts,), jnp.float32, smallest / len(cuts), largest / len(cuts)))
        gain = gain * jnp.repeat(draws, shape[dim] // parts).reshape([-1 if axis == dim else 1 for axis in range(len(shape))])
    return gain


def normal_values(own_key, extent, width, most, pieces=(), kind=jnp.bfloat16):
    result = jax.random.normal(own_key, extent, jnp.float32) * width
    if len(pieces) > 0:
        result = block_levels(own_key, extent, pieces, -0.22, 0.18) * result
    return jnp.clip(result, min=-most, max=most).astype(kind)


def setup_inputs(seed: int = 0) -> dict:
    streams_of = jax.random.split(jax.random.key(seed), 9)
    return {
        "tokens": normal_values(streams_of[0], (TOKENS, D), 1.0, 6.0, ((0, 64), (1, 8))),
        "route_ids": draw_route_ids(jax.random.fold_in(streams_of[8], 71), 0),
        "route_slots": draw_route_slots(jax.random.fold_in(streams_of[8], 71), 0),
        "keep_mask": draw_keep_mask(jax.random.fold_in(streams_of[8], 71), 0),
        "route_weights": jnp.clip(0.05 + 0.55 * jax.random.uniform(streams_of[4], (TOKENS, TOPK), jnp.float32) ** block_levels(streams_of[4], (TOKENS, TOPK), ((0, 64),), -0.2, 0.2), 0.05, 0.6),
        "gate_weight": normal_values(streams_of[5], (EXPERT_TOTAL, D, HID), D ** -0.5, 0.09375, ((0, 64), (2, 8))),
        "up_weight": normal_values(streams_of[6], (EXPERT_TOTAL, D, HID), D ** -0.5, 0.09375, ((0, 64), (2, 8))),
        "down_weight": normal_values(streams_of[7], (EXPERT_TOTAL, HID, D), HID ** -0.5, 0.1875, ((0, 64), (2, 8))),
    }


def reference(tokens, route_ids, route_slots, keep_mask, route_weights, gate_weight, up_weight, down_weight):
    blocks = TOKENS // TOK_G
    span = blocks * SLOT_LIMIT
    slots_all = EXPERT_TOTAL * span
    token_index = jnp.arange(TOKENS, dtype=jnp.int32)
    group_index = (token_index // TOK_G).astype(jnp.int32)[:, None]
    position = (route_ids * span + group_index * SLOT_LIMIT + route_slots).astype(jnp.int32)
    is_kept = keep_mask > 0
    target = jnp.where(is_kept, position, slots_all).astype(jnp.int32)
    token_grid = jnp.broadcast_to(token_index[:, None], position.shape)
    owner = jnp.full((slots_all,), -1, jnp.int32).at[target.reshape(-1)].set(token_grid.reshape(-1), mode="drop")
    owner = owner.reshape(EXPERT_TOTAL, span)

    def one_expert(packed):
        source, gate_matrix, up_matrix, down_matrix = packed
        picked_rows = tokens[jnp.maximum(source, 0).astype(jnp.int32)]
        expert_rows = jnp.where((source >= 0)[:, None], picked_rows, jnp.zeros((), tokens.dtype))
        gate_value = jnp.dot(expert_rows, gate_matrix, preferred_element_type=jnp.float32)
        up_value = jnp.dot(expert_rows, up_matrix, preferred_element_type=jnp.float32)
        hidden = (jax.nn.silu(gate_value) * up_value).astype(jnp.bfloat16)
        return jnp.dot(hidden, down_matrix, preferred_element_type=jnp.float32).astype(jnp.bfloat16)

    outputs = lax.map(one_expert, (owner, gate_weight, up_weight, down_weight)).reshape(slots_all, D)
    weights_kept = jnp.where(is_kept, route_weights, jnp.zeros((), jnp.float32))
    combined = jnp.zeros((TOKENS, D), jnp.float32)
    for route in range(TOPK):
        combined = combined + weights_kept[:, route:route + 1] * outputs[position[:, route]].astype(jnp.float32)
    return combined.astype(jnp.bfloat16)
```

```python
import jax
import jax.numpy as jnp
from jax import lax
from jax.sharding import PartitionSpec as P


def body(
    tokens, route_ids, route_slots, keep_mask, route_weights, gate_weight, up_weight, down_weight
):
    groups = lax.axis_size("node")
    tok_rows = tokens.shape[0]
    top_count = route_ids.shape[1]
    capacity = (5 * tok_rows * top_count + 4 * groups - 1) // (4 * groups)
    slots_all = groups * capacity
    is_kept = keep_mask > 0
    position = route_ids * capacity + route_slots
    target = jnp.where(is_kept, position, slots_all)
    token_grid = jnp.broadcast_to(jnp.arange(tok_rows, dtype=jnp.int32)[:, None], position.shape)
    owner = (
        jnp.full((slots_all,), -1, jnp.int32)
        .at[target.reshape(-1)]
        .set(token_grid.reshape(-1), mode="drop")
    )
    filled = (owner >= 0)[:, None]
    owner_row = jnp.maximum(owner, 0)
    gate_matrix = gate_weight[0]
    up_matrix = up_weight[0]
    down_matrix = down_weight[0]
    outgoing = jnp.where(filled, tokens[owner_row], jnp.zeros((), tokens.dtype))
    outgoing = outgoing.reshape(groups, capacity, tokens.shape[1])
    arrived = lax.all_to_all(outgoing, "node", split_axis=0, concat_axis=0, tiled=True)
    slot_count = arrived.shape[1]
    shard_rows = arrived.reshape(groups * slot_count, arrived.shape[2])
    flat_rows = lax.all_gather(shard_rows, "local", axis=1, tiled=True)
    gate_value = jnp.dot(flat_rows, gate_matrix, preferred_element_type=jnp.float32)
    up_value = jnp.dot(flat_rows, up_matrix, preferred_element_type=jnp.float32)
    hidden = (jax.nn.silu(gate_value) * up_value).astype(jnp.bfloat16)
    expert_out = jnp.dot(
        lax.all_gather(hidden, "local", axis=1, tiled=True),
        down_matrix,
        preferred_element_type=jnp.float32,
    )
    expert_out = expert_out.astype(jnp.bfloat16).reshape(groups, slot_count, down_matrix.shape[1])
    returned_rows = lax.all_to_all(expert_out, "node", split_axis=0, concat_axis=0, tiled=True)
    flat_back = returned_rows.reshape(slots_all, returned_rows.shape[2])
    weights_kept = jnp.where(is_kept, route_weights, jnp.zeros((), jnp.float32))
    mixed = jnp.zeros((tok_rows, flat_back.shape[1]), jnp.float32)
    for route in range(top_count):
        mixed = mixed + weights_kept[:, route : route + 1] * flat_back[position[:, route]].astype(
            jnp.float32
        )
    return mixed.astype(jnp.bfloat16)


def solution(mesh):
    in_specs = (
        P("node", "local"),
        P("node", None),
        P("node", None),
        P("node", None),
        P("node", None),
        P("node", None, "local"),
        P("node", None, "local"),
        P("node", None, "local"),
    )
    out_specs = P("node", "local")
    return jax.shard_map(body, mesh=mesh, in_specs=in_specs, out_specs=out_specs, check_vma=False)
```

```python
import jax
import jax.numpy as jnp
from jax import lax
from jax.sharding import Mesh
from jax.sharding import PartitionSpec as P


def node_all_to_all(x, outer, inner):
    inner_size = lax.axis_size(inner)
    y = x.reshape(x.shape[0] // inner_size, inner_size, *x.shape[1:])
    y = lax.all_to_all(y, inner, 1, 1, tiled=True)
    y = lax.all_to_all(y, outer, 0, 0, tiled=True)
    return y.reshape(x.shape)


def local_all_gather(x, axis_name):
    count = lax.axis_size(axis_name)
    copies = jnp.broadcast_to(x[None], (count,) + x.shape)
    got = lax.all_to_all(copies, axis_name, 0, 0, tiled=True)
    return jnp.moveaxis(got, 0, 1).reshape(x.shape[0], count * x.shape[1])


def make_body(outer, inner):
    node = (outer, inner)

    def body(
        tokens, route_ids, route_slots, keep_mask, route_weights, gate_weight, up_weight, down_weight
    ):
        groups = lax.axis_size(node)
        tok_rows = tokens.shape[0]
        top_count = route_ids.shape[1]
        capacity = (5 * tok_rows * top_count + 4 * groups - 1) // (4 * groups)
        slots_all = groups * capacity
        is_kept = keep_mask > 0
        position = route_ids * capacity + route_slots
        target = jnp.where(is_kept, position, slots_all)
        token_grid = jnp.broadcast_to(jnp.arange(tok_rows, dtype=jnp.int32)[:, None], position.shape)
        owner = (
            jnp.full((slots_all,), -1, jnp.int32)
            .at[target.reshape(-1)]
            .set(token_grid.reshape(-1), mode="drop")
        )
        filled = (owner >= 0)[:, None]
        owner_row = jnp.maximum(owner, 0)
        gate_matrix = gate_weight[0]
        up_matrix = up_weight[0]
        down_matrix = down_weight[0]
        outgoing = jnp.where(filled, tokens[owner_row], jnp.zeros((), tokens.dtype))
        outgoing = outgoing.reshape(groups, capacity, tokens.shape[1])
        arrived = node_all_to_all(outgoing, outer, inner)
        slot_count = arrived.shape[1]
        shard_rows = arrived.reshape(groups * slot_count, arrived.shape[2])
        flat_rows = lax.all_gather(shard_rows, "local", axis=1, tiled=True)
        gate_value = jnp.dot(flat_rows, gate_matrix, preferred_element_type=jnp.float32)
        up_value = jnp.dot(flat_rows, up_matrix, preferred_element_type=jnp.float32)
        hidden = (jax.nn.silu(gate_value) * up_value).astype(jnp.bfloat16)
        expert_out = jnp.dot(
            local_all_gather(hidden, "local"),
            down_matrix,
            preferred_element_type=jnp.float32,
        )
        expert_out = expert_out.astype(jnp.bfloat16).reshape(groups, slot_count, down_matrix.shape[1])
        returned_rows = node_all_to_all(expert_out, outer, inner)
        flat_back = returned_rows.reshape(slots_all, returned_rows.shape[2])
        weights_kept = jnp.where(is_kept, route_weights, jnp.zeros((), jnp.float32))
        mixed = jnp.zeros((tok_rows, flat_back.shape[1]), jnp.float32)
        for route in range(top_count):
            mixed = mixed + weights_kept[:, route : route + 1] * flat_back[position[:, route]].astype(
                jnp.float32
            )
        return mixed.astype(jnp.bfloat16)

    return body


def solution(mesh):
    outer_size = mesh.devices.shape[0] // 4 if mesh.devices.shape[0] % 4 == 0 else mesh.devices.shape[0]
    inner_size = mesh.devices.shape[0] // outer_size
    split = Mesh(
        mesh.devices.reshape(outer_size, inner_size, *mesh.devices.shape[1:]),
        ("node_outer", "node_inner", "local"),
    )
    node = ("node_outer", "node_inner")
    in_specs = (
        P(node, "local"),
        P(node, None),
        P(node, None),
        P(node, None),
        P(node, None),
        P(node, None, "local"),
        P(node, None, "local"),
        P(node, None, "local"),
    )
    out_specs = P(node, "local")
    return jax.shard_map(
        make_body("node_outer", "node_inner"),
        mesh=split,
        in_specs=in_specs,
        out_specs=out_specs,
        check_vma=False,
    )
```

```python
import jax
import jax.numpy as jnp
from jax import lax
from jax.sharding import Mesh
from jax.sharding import PartitionSpec as P


def node_all_to_all(x, outer, inner):
    inner_size = lax.axis_size(inner)
    y = x.reshape(x.shape[0] // inner_size, inner_size, *x.shape[1:])
    y = lax.all_to_all(y, inner, 1, 1, tiled=True)
    y = lax.all_to_all(y, outer, 0, 0, tiled=True)
    return y.reshape(x.shape)


def local_all_gather(x, axis_name):
    count = lax.axis_size(axis_name)
    copies = jnp.broadcast_to(x[None], (count,) + x.shape)
    got = lax.all_to_all(copies, axis_name, 0, 0, tiled=True)
    return jnp.moveaxis(got, 0, 1).reshape(x.shape[0], count * x.shape[1])


def make_body(outer, inner):
    node = (outer, inner)

    def body(
        tokens, route_ids, route_slots, keep_mask, route_weights, gate_weight, up_weight, down_weight
    ):
        groups = lax.axis_size(node)
        tok_rows = tokens.shape[0]
        top_count = route_ids.shape[1]
        capacity = (5 * tok_rows * top_count + 4 * groups - 1) // (4 * groups)
        slots_all = groups * capacity
        is_kept = keep_mask > 0
        position = route_ids * capacity + route_slots
        target = jnp.where(is_kept, position, slots_all)
        token_grid = jnp.broadcast_to(jnp.arange(tok_rows, dtype=jnp.int32)[:, None], position.shape)
        owner = (
            jnp.full((slots_all,), -1, jnp.int32)
            .at[target.reshape(-1)]
            .set(token_grid.reshape(-1), mode="drop")
        )
        filled = (owner >= 0)[:, None]
        owner_row = jnp.maximum(owner, 0)
        gate_matrix = gate_weight[0]
        up_matrix = up_weight[0]
        down_matrix = down_weight[0]
        outgoing = jnp.where(filled, tokens[owner_row], jnp.zeros((), tokens.dtype))
        outgoing = outgoing.reshape(groups, capacity, tokens.shape[1])
        chunk_count = 2 if capacity % 2 == 0 else 1
        chunk = capacity // chunk_count
        returned = []
        for part in range(chunk_count):
            arrived = node_all_to_all(outgoing[:, part * chunk : (part + 1) * chunk], outer, inner)
            shard_rows = arrived.reshape(groups * chunk, arrived.shape[2])
            flat_rows = lax.all_gather(shard_rows, "local", axis=1, tiled=True)
            gate_value = jnp.dot(flat_rows, gate_matrix, preferred_element_type=jnp.float32)
            up_value = jnp.dot(flat_rows, up_matrix, preferred_element_type=jnp.float32)
            hidden = (jax.nn.silu(gate_value) * up_value).astype(jnp.bfloat16)
            expert_out = jnp.dot(
                local_all_gather(hidden, "local"),
                down_matrix,
                preferred_element_type=jnp.float32,
            )
            expert_out = expert_out.astype(jnp.bfloat16).reshape(groups, chunk, down_matrix.shape[1])
            returned.append(node_all_to_all(expert_out, outer, inner))
        returned_rows = jnp.concatenate(returned, axis=1)
        flat_back = returned_rows.reshape(slots_all, returned_rows.shape[2])
        weights_kept = jnp.where(is_kept, route_weights, jnp.zeros((), jnp.float32))
        mixed = jnp.zeros((tok_rows, flat_back.shape[1]), jnp.float32)
        for route in range(top_count):
            mixed = mixed + weights_kept[:, route : route + 1] * flat_back[position[:, route]].astype(
                jnp.float32
            )
        return mixed.astype(jnp.bfloat16)

    return body


def solution(mesh):
    outer_size = mesh.devices.shape[0] // 4 if mesh.devices.shape[0] % 4 == 0 else mesh.devices.shape[0]
    inner_size = mesh.devices.shape[0] // outer_size
    split = Mesh(
        mesh.devices.reshape(outer_size, inner_size, *mesh.devices.shape[1:]),
        ("node_outer", "node_inner", "local"),
    )
    node = ("node_outer", "node_inner")
    in_specs = (
        P(node, "local"),
        P(node, None),
        P(node, None),
        P(node, None),
        P(node, None),
        P(node, None, "local"),
        P(node, None, "local"),
        P(node, None, "local"),
    )
    out_specs = P(node, "local")
    return jax.shard_map(
        make_body("node_outer", "node_inner"),
        mesh=split,
        in_specs=in_specs,
        out_specs=out_specs,
        check_vma=False,
    )
```

```python
import jax
import jax.numpy as jnp
from jax import lax
from jax.sharding import Mesh
from jax.sharding import PartitionSpec as P


def node_all_to_all(x, outer, inner):
    inner_size = lax.axis_size(inner)
    y = x.reshape(x.shape[0] // inner_size, inner_size, *x.shape[1:])
    y = lax.all_to_all(y, inner, 1, 1, tiled=True)
    y = lax.all_to_all(y, outer, 0, 0, tiled=True)
    return y.reshape(x.shape)


def local_all_gather(x, axis_name):
    count = lax.axis_size(axis_name)
    copies = jnp.broadcast_to(x[None], (count,) + x.shape)
    return lax.all_to_all(copies, axis_name, 0, 0, tiled=True)


def make_body(outer, inner):
    node = (outer, inner)

    def body(
        tokens, route_ids, route_slots, keep_mask, route_weights, gate_weight, up_weight, down_weight
    ):
        groups = lax.axis_size(node)
        tok_rows = tokens.shape[0]
        top_count = route_ids.shape[1]
        capacity = (5 * tok_rows * top_count + 4 * groups - 1) // (4 * groups)
        slots_all = groups * capacity
        is_kept = keep_mask > 0
        position = route_ids * capacity + route_slots
        target = jnp.where(is_kept, position, slots_all)
        slot_index = jnp.arange(slots_all, dtype=jnp.int32)
        dispatch = jnp.zeros((slots_all, tok_rows), jnp.bfloat16)
        for route in range(top_count):
            dispatch = dispatch + (slot_index[:, None] == target[None, :, route]).astype(jnp.bfloat16)
        gate_matrix = gate_weight[0]
        up_matrix = up_weight[0]
        down_matrix = down_weight[0]
        outgoing = jnp.dot(dispatch, tokens, preferred_element_type=jnp.float32).astype(tokens.dtype)
        outgoing = outgoing.reshape(groups, capacity, tokens.shape[1])
        arrived = node_all_to_all(outgoing, outer, inner)
        slot_count = arrived.shape[1]
        shard_rows = arrived.reshape(groups * slot_count, arrived.shape[2])
        flat_rows = lax.all_gather(shard_rows, "local", axis=1, tiled=True)
        gate_value = jnp.dot(flat_rows, gate_matrix, preferred_element_type=jnp.float32)
        up_value = jnp.dot(flat_rows, up_matrix, preferred_element_type=jnp.float32)
        hidden = (jax.nn.silu(gate_value) * up_value).astype(jnp.bfloat16)
        hidden_parts = local_all_gather(hidden, "local")
        expert_out = jnp.einsum(
            "lrh,lhd->rd",
            hidden_parts,
            down_matrix.reshape(hidden_parts.shape[0], hidden.shape[1], down_matrix.shape[1]),
            preferred_element_type=jnp.float32,
        )
        expert_out = expert_out.astype(jnp.bfloat16).reshape(groups, slot_count, down_matrix.shape[1])
        returned_rows = node_all_to_all(expert_out, outer, inner)
        flat_back = returned_rows.reshape(slots_all, returned_rows.shape[2])
        weights_kept = jnp.where(is_kept, route_weights, jnp.zeros((), jnp.float32))
        combine = jnp.zeros((tok_rows, slots_all), jnp.float32)
        for route in range(top_count):
            combine = combine + jnp.where(
                position[:, route : route + 1] == slot_index[None, :], weights_kept[:, route : route + 1], 0.0
            )
        mixed = jnp.dot(
            combine,
            flat_back.astype(jnp.float32),
            precision=lax.Precision.HIGHEST,
            preferred_element_type=jnp.float32,
        )
        return mixed.astype(jnp.bfloat16)

    return body


def solution(mesh):
    outer_size = mesh.devices.shape[0] // 4 if mesh.devices.shape[0] % 4 == 0 else mesh.devices.shape[0]
    inner_size = mesh.devices.shape[0] // outer_size
    split = Mesh(
        mesh.devices.reshape(outer_size, inner_size, *mesh.devices.shape[1:]),
        ("node_outer", "node_inner", "local"),
    )
    node = ("node_outer", "node_inner")
    in_specs = (
        P(node, "local"),
        P(node, None),
        P(node, None),
        P(node, None),
        P(node, None),
        P(node, None, "local"),
        P(node, None, "local"),
        P(node, None, "local"),
    )
    out_specs = P(node, "local")
    return jax.shard_map(
        make_body("node_outer", "node_inner"),
        mesh=split,
        in_specs=in_specs,
        out_specs=out_specs,
        check_vma=False,
    )
```

```python
import jax
import jax.numpy as jnp
from jax import lax
from jax.sharding import Mesh
from jax.sharding import PartitionSpec as P


def node_all_to_all(x, outer, inner):
    inner_size = lax.axis_size(inner)
    y = x.reshape(x.shape[0] // inner_size, inner_size, *x.shape[1:])
    y = lax.all_to_all(y, inner, 1, 1, tiled=True)
    y = lax.all_to_all(y, outer, 0, 0, tiled=True)
    return y.reshape(x.shape)


def local_all_gather(x, axis_name):
    count = lax.axis_size(axis_name)
    copies = jnp.broadcast_to(x[None], (count,) + x.shape)
    return lax.all_to_all(copies, axis_name, 0, 0, tiled=True)


def make_body(outer, inner):
    node = (outer, inner)

    def body(
        tokens, route_ids, route_slots, keep_mask, route_weights, gate_weight, up_weight, down_weight
    ):
        groups = lax.axis_size(node)
        tok_rows = tokens.shape[0]
        top_count = route_ids.shape[1]
        capacity = (5 * tok_rows * top_count + 4 * groups - 1) // (4 * groups)
        slots_all = groups * capacity
        is_kept = keep_mask > 0
        position = route_ids * capacity + route_slots
        target = jnp.where(is_kept, position, slots_all)
        slot_index = jnp.arange(slots_all, dtype=jnp.int32)
        dispatch = jnp.zeros((slots_all, tok_rows), jnp.bfloat16)
        for route in range(top_count):
            dispatch = dispatch + (slot_index[:, None] == target[None, :, route]).astype(jnp.bfloat16)
        gate_matrix = gate_weight[0]
        up_matrix = up_weight[0]
        down_matrix = down_weight[0]
        outgoing = jnp.dot(dispatch, tokens, preferred_element_type=jnp.float32).astype(tokens.dtype)
        outgoing = outgoing.reshape(groups, capacity, tokens.shape[1])
        arrived = node_all_to_all(outgoing, outer, inner)
        slot_count = arrived.shape[1]
        shard_rows = arrived.reshape(groups * slot_count, arrived.shape[2])
        chip_rows = local_all_gather(shard_rows, "local_chip")
        row_parts = local_all_gather(chip_rows, "local_core")
        chips, cores = chip_rows.shape[0], row_parts.shape[0]
        feature = shard_rows.shape[1]

        def by_part(matrix):
            return jnp.swapaxes(matrix.reshape(chips, cores, feature, matrix.shape[1]), 0, 1)

        gate_value = jnp.einsum(
            "cyrd,cydh->rh", row_parts, by_part(gate_matrix), preferred_element_type=jnp.float32
        )
        up_value = jnp.einsum(
            "cyrd,cydh->rh", row_parts, by_part(up_matrix), preferred_element_type=jnp.float32
        )
        hidden = (jax.nn.silu(gate_value) * up_value).astype(jnp.bfloat16)
        hidden_parts = local_all_gather(hidden, ("local_chip", "local_core"))
        expert_out = jnp.einsum(
            "lrh,lhd->rd",
            hidden_parts,
            down_matrix.reshape(hidden_parts.shape[0], hidden.shape[1], down_matrix.shape[1]),
            preferred_element_type=jnp.float32,
        )
        expert_out = expert_out.astype(jnp.bfloat16).reshape(groups, slot_count, down_matrix.shape[1])
        returned_rows = node_all_to_all(expert_out, outer, inner)
        flat_back = returned_rows.reshape(slots_all, returned_rows.shape[2])
        weights_kept = jnp.where(is_kept, route_weights, jnp.zeros((), jnp.float32))
        combine = jnp.zeros((tok_rows, slots_all), jnp.float32)
        for route in range(top_count):
            combine = combine + jnp.where(
                position[:, route : route + 1] == slot_index[None, :], weights_kept[:, route : route + 1], 0.0
            )
        mixed = jnp.dot(
            combine,
            flat_back.astype(jnp.float32),
            precision=lax.Precision.HIGHEST,
            preferred_element_type=jnp.float32,
        )
        return mixed.astype(jnp.bfloat16)

    return body


def solution(mesh):
    outer_size = mesh.devices.shape[0] // 4 if mesh.devices.shape[0] % 4 == 0 else mesh.devices.shape[0]
    inner_size = mesh.devices.shape[0] // outer_size
    local_size = mesh.devices.shape[1]
    core_size = 2 if local_size % 2 == 0 else 1
    split = Mesh(
        mesh.devices.reshape(outer_size, inner_size, local_size // core_size, core_size),
        ("node_outer", "node_inner", "local_chip", "local_core"),
    )
    node = ("node_outer", "node_inner")
    local = ("local_chip", "local_core")
    in_specs = (
        P(node, local),
        P(node, None),
        P(node, None),
        P(node, None),
        P(node, None),
        P(node, None, local),
        P(node, None, local),
        P(node, None, local),
    )
    out_specs = P(node, local)
    return jax.shard_map(
        make_body("node_outer", "node_inner"),
        mesh=split,
        in_specs=in_specs,
        out_specs=out_specs,
        check_vma=False,
    )
```

```python
import jax
import jax.numpy as jnp
from jax import lax
from jax.sharding import Mesh
from jax.sharding import PartitionSpec as P


def node_all_to_all(x, outer, inner):
    inner_size = lax.axis_size(inner)
    y = x.reshape(x.shape[0] // inner_size, inner_size, *x.shape[1:])
    y = lax.all_to_all(y, inner, 1, 1, tiled=True)
    y = lax.all_to_all(y, outer, 0, 0, tiled=True)
    return y.reshape(x.shape)


def local_all_gather(x, axis_name):
    count = lax.axis_size(axis_name)
    copies = jnp.broadcast_to(x[None], (count,) + x.shape)
    return lax.all_to_all(copies, axis_name, 0, 0, tiled=True)


def make_body(outer, inner):
    node = (outer, inner)

    def body(
        tokens, route_ids, route_slots, keep_mask, route_weights, gate_weight, up_weight, down_weight
    ):
        groups = lax.axis_size(node)
        tok_rows = tokens.shape[0]
        top_count = route_ids.shape[1]
        capacity = (5 * tok_rows * top_count + 4 * groups - 1) // (4 * groups)
        slots_all = groups * capacity
        is_kept = keep_mask > 0
        position = route_ids * capacity + route_slots
        target = jnp.where(is_kept, position, slots_all)
        slot_index = jnp.arange(slots_all, dtype=jnp.int32)
        dispatch = jnp.zeros((slots_all, tok_rows), jnp.bfloat16)
        for route in range(top_count):
            dispatch = dispatch + (slot_index[:, None] == target[None, :, route]).astype(jnp.bfloat16)
        gate_matrix = gate_weight[0]
        up_matrix = up_weight[0]
        down_matrix = down_weight[0]
        outgoing = jnp.dot(dispatch, tokens, preferred_element_type=jnp.float32).astype(tokens.dtype)
        outgoing = outgoing.reshape(groups, capacity, tokens.shape[1])
        arrived = node_all_to_all(outgoing, outer, inner)
        slot_count = arrived.shape[1]
        shard_rows = arrived.reshape(groups * slot_count, arrived.shape[2])
        chip_rows = local_all_gather(shard_rows, "local_chip")
        row_parts = local_all_gather(chip_rows, "local_core")
        chips, cores = chip_rows.shape[0], row_parts.shape[0]
        feature = shard_rows.shape[1]

        def by_part(matrix):
            return jnp.swapaxes(matrix.reshape(chips, cores, feature, matrix.shape[1]), 0, 1)

        gate_value = jnp.einsum(
            "cyrd,cydh->rh", row_parts, by_part(gate_matrix), preferred_element_type=jnp.float32
        )
        up_value = jnp.einsum(
            "cyrd,cydh->rh", row_parts, by_part(up_matrix), preferred_element_type=jnp.float32
        )
        hidden = (jax.nn.silu(gate_value) * up_value).astype(jnp.bfloat16)
        hidden_parts = local_all_gather(local_all_gather(hidden, "local_chip"), "local_core")
        down_parts = jnp.swapaxes(
            down_matrix.reshape(chips, cores, hidden.shape[1], down_matrix.shape[1]), 0, 1
        )
        expert_out = jnp.einsum(
            "cyrh,cyhd->rd", hidden_parts, down_parts, preferred_element_type=jnp.float32
        )
        expert_out = expert_out.astype(jnp.bfloat16).reshape(groups, slot_count, down_matrix.shape[1])
        returned_rows = node_all_to_all(expert_out, outer, inner)
        flat_back = returned_rows.reshape(slots_all, returned_rows.shape[2])
        weights_kept = jnp.where(is_kept, route_weights, jnp.zeros((), jnp.float32))
        combine = jnp.zeros((tok_rows, slots_all), jnp.float32)
        for route in range(top_count):
            combine = combine + jnp.where(
                position[:, route : route + 1] == slot_index[None, :], weights_kept[:, route : route + 1], 0.0
            )
        mixed = jnp.dot(
            combine,
            flat_back.astype(jnp.float32),
            precision=lax.Precision.HIGHEST,
            preferred_element_type=jnp.float32,
        )
        return mixed.astype(jnp.bfloat16)

    return body


def solution(mesh):
    outer_size = mesh.devices.shape[0] // 4 if mesh.devices.shape[0] % 4 == 0 else mesh.devices.shape[0]
    inner_size = mesh.devices.shape[0] // outer_size
    local_size = mesh.devices.shape[1]
    core_size = 2 if local_size % 2 == 0 else 1
    split = Mesh(
        mesh.devices.reshape(outer_size, inner_size, local_size // core_size, core_size),
        ("node_outer", "node_inner", "local_chip", "local_core"),
    )
    node = ("node_outer", "node_inner")
    local = ("local_chip", "local_core")
    in_specs = (
        P(node, local),
        P(node, None),
        P(node, None),
        P(node, None),
        P(node, None),
        P(node, None, local),
        P(node, None, local),
        P(node, None, local),
    )
    out_specs = P(node, local)
    return jax.shard_map(
        make_body("node_outer", "node_inner"),
        mesh=split,
        in_specs=in_specs,
        out_specs=out_specs,
        check_vma=False,
    )
```

```python
import jax
import jax.numpy as jnp
from jax import lax
from jax.sharding import Mesh
from jax.sharding import PartitionSpec as P


def node_all_to_all(x, outer, inner):
    inner_size = lax.axis_size(inner)
    y = x.reshape(x.shape[0] // inner_size, inner_size, *x.shape[1:])
    y = lax.all_to_all(y, inner, 1, 1, tiled=True)
    y = lax.all_to_all(y, outer, 0, 0, tiled=True)
    return y.reshape(x.shape)


def local_all_gather(x, axis_name):
    count = lax.axis_size(axis_name)
    copies = jnp.broadcast_to(x[None], (count,) + x.shape)
    return lax.all_to_all(copies, axis_name, 0, 0, tiled=True)


def make_body(outer, inner):
    node = (outer, inner)

    def body(
        tokens, route_ids, route_slots, keep_mask, route_weights, gate_weight, up_weight, down_weight
    ):
        groups = lax.axis_size(node)
        tok_rows = tokens.shape[0]
        top_count = route_ids.shape[1]
        capacity = (5 * tok_rows * top_count + 4 * groups - 1) // (4 * groups)
        slots_all = groups * capacity
        is_kept = keep_mask > 0
        position = route_ids * capacity + route_slots
        target = jnp.where(is_kept, position, slots_all)
        slot_index = jnp.arange(slots_all, dtype=jnp.int32)
        dispatch = jnp.zeros((slots_all, tok_rows), jnp.bfloat16)
        for route in range(top_count):
            dispatch = dispatch + (slot_index[:, None] == target[None, :, route]).astype(jnp.bfloat16)
        gate_matrix = gate_weight[0]
        up_matrix = up_weight[0]
        down_matrix = down_weight[0]
        outgoing = jnp.dot(dispatch, tokens, preferred_element_type=jnp.float32).astype(tokens.dtype)
        outgoing = outgoing.reshape(groups, capacity, tokens.shape[1])
        outer_size = lax.axis_size(outer)
        inner_size = lax.axis_size(inner)
        chips = lax.axis_size("local_chip")
        cores = lax.axis_size("local_core")
        feature = tokens.shape[1]
        by_outer = outgoing.reshape(outer_size, inner_size, capacity, feature)
        by_outer = lax.all_to_all(by_outer, outer, 0, 0, tiled=True)
        copies = jnp.broadcast_to(
            jnp.swapaxes(by_outer, 0, 1)[:, None],
            (inner_size, chips, outer_size, capacity, feature),
        ).reshape(inner_size * chips, outer_size, capacity, feature)
        chip_rows = lax.all_to_all(copies, (inner, "local_chip"), 0, 0, tiled=True)
        chip_rows = chip_rows.reshape(inner_size, chips, outer_size, capacity, feature)
        row_parts = local_all_gather(chip_rows, "local_core")
        slot_count = capacity

        def by_part(matrix):
            return jnp.swapaxes(matrix.reshape(chips, cores, feature, matrix.shape[1]), 0, 1)

        gate_value = jnp.einsum(
            "cxyzsd,cydh->xzsh", row_parts, by_part(gate_matrix), preferred_element_type=jnp.float32
        ).reshape(groups * slot_count, gate_matrix.shape[1])
        up_value = jnp.einsum(
            "cxyzsd,cydh->xzsh", row_parts, by_part(up_matrix), preferred_element_type=jnp.float32
        ).reshape(groups * slot_count, up_matrix.shape[1])
        hidden = (jax.nn.silu(gate_value) * up_value).astype(jnp.bfloat16)
        hidden_parts = local_all_gather(local_all_gather(hidden, "local_chip"), "local_core")
        down_parts = jnp.swapaxes(
            down_matrix.reshape(chips, cores, hidden.shape[1], down_matrix.shape[1]), 0, 1
        )
        expert_out = jnp.einsum(
            "cyrh,cyhd->rd", hidden_parts, down_parts, preferred_element_type=jnp.float32
        )
        expert_out = expert_out.astype(jnp.bfloat16).reshape(
            inner_size, outer_size, slot_count, down_matrix.shape[1]
        )
        returned_rows = lax.all_to_all(expert_out, inner, 0, 0, tiled=True)
        returned_rows = lax.all_to_all(returned_rows, outer, 1, 1, tiled=True)
        flat_back = returned_rows.reshape(slots_all, returned_rows.shape[-1])
        back_position = (
            (route_ids % inner_size) * (outer_size * capacity) + (route_ids // inner_size) * capacity + route_slots
        )
        weights_kept = jnp.where(is_kept, route_weights, jnp.zeros((), jnp.float32))
        combine = jnp.zeros((tok_rows, slots_all), jnp.float32)
        for route in range(top_count):
            combine = combine + jnp.where(
                back_position[:, route : route + 1] == slot_index[None, :], weights_kept[:, route : route + 1], 0.0
            )
        mixed = jnp.dot(
            combine,
            flat_back.astype(jnp.float32),
            precision=lax.Precision.HIGHEST,
            preferred_element_type=jnp.float32,
        )
        return mixed.astype(jnp.bfloat16)

    return body


def solution(mesh):
    outer_size = mesh.devices.shape[0] // 4 if mesh.devices.shape[0] % 4 == 0 else mesh.devices.shape[0]
    inner_size = mesh.devices.shape[0] // outer_size
    local_size = mesh.devices.shape[1]
    core_size = 2 if local_size % 2 == 0 else 1
    split = Mesh(
        mesh.devices.reshape(outer_size, inner_size, local_size // core_size, core_size),
        ("node_outer", "node_inner", "local_chip", "local_core"),
    )
    node = ("node_outer", "node_inner")
    local = ("local_chip", "local_core")
    in_specs = (
        P(node, local),
        P(node, None),
        P(node, None),
        P(node, None),
        P(node, None),
        P(node, None, local),
        P(node, None, local),
        P(node, None, local),
    )
    out_specs = P(node, local)
    return jax.shard_map(
        make_body("node_outer", "node_inner"),
        mesh=split,
        in_specs=in_specs,
        out_specs=out_specs,
        check_vma=False,
    )
```

```python
import jax
import jax.numpy as jnp
from jax import lax
from jax.sharding import Mesh
from jax.sharding import PartitionSpec as P


def node_all_to_all(x, outer, inner):
    inner_size = lax.axis_size(inner)
    y = x.reshape(x.shape[0] // inner_size, inner_size, *x.shape[1:])
    y = lax.all_to_all(y, inner, 1, 1, tiled=True)
    y = lax.all_to_all(y, outer, 0, 0, tiled=True)
    return y.reshape(x.shape)


def local_all_gather(x, axis_name):
    count = lax.axis_size(axis_name)
    copies = jnp.broadcast_to(x[None], (count,) + x.shape)
    return lax.all_to_all(copies, axis_name, 0, 0, tiled=True)


def make_body(outer, inner):
    node = (outer, inner)

    def body(
        tokens, route_ids, route_slots, keep_mask, route_weights, gate_weight, up_weight, down_weight
    ):
        groups = lax.axis_size(node)
        tok_rows = tokens.shape[0]
        top_count = route_ids.shape[1]
        capacity = (5 * tok_rows * top_count + 4 * groups - 1) // (4 * groups)
        slots_all = groups * capacity
        is_kept = keep_mask > 0
        position = route_ids * capacity + route_slots
        target = jnp.where(is_kept, position, slots_all)
        slot_index = jnp.arange(slots_all, dtype=jnp.int32)
        dispatch = jnp.zeros((slots_all, tok_rows), jnp.bfloat16)
        for route in range(top_count):
            dispatch = dispatch + (slot_index[:, None] == target[None, :, route]).astype(jnp.bfloat16)
        gate_matrix = gate_weight[0]
        up_matrix = up_weight[0]
        down_matrix = down_weight[0]
        outgoing = jnp.dot(dispatch, tokens, preferred_element_type=jnp.float32).astype(tokens.dtype)
        outgoing = outgoing.reshape(groups, capacity, tokens.shape[1])
        outer_size = lax.axis_size(outer)
        inner_size = lax.axis_size(inner)
        chips = lax.axis_size("local_chip")
        cores = lax.axis_size("local_core")
        feature = tokens.shape[1]
        by_outer = outgoing.reshape(outer_size, inner_size, capacity, feature)
        by_outer = lax.all_to_all(by_outer, outer, 0, 0, tiled=True)
        copies = jnp.broadcast_to(
            jnp.swapaxes(by_outer, 0, 1)[:, None],
            (inner_size, chips, outer_size, capacity, feature),
        ).reshape(inner_size * chips, outer_size, capacity, feature)
        chip_rows = lax.all_to_all(copies, (inner, "local_chip"), 0, 0, tiled=True)
        chip_rows = chip_rows.reshape(inner_size, chips, outer_size, capacity, feature)
        row_parts = local_all_gather(chip_rows, "local_core")
        slot_count = capacity

        def by_part(matrix):
            return jnp.swapaxes(matrix.reshape(chips, cores, feature, matrix.shape[1]), 0, 1)

        both_value = jnp.einsum(
            "cxyzsd,cydh->xzsh",
            row_parts,
            by_part(jnp.concatenate([gate_matrix, up_matrix], axis=1)),
            preferred_element_type=jnp.float32,
        ).reshape(groups * slot_count, 2 * gate_matrix.shape[1])
        gate_value = both_value[:, : gate_matrix.shape[1]]
        up_value = both_value[:, gate_matrix.shape[1] :]
        hidden = (jax.nn.silu(gate_value) * up_value).astype(jnp.bfloat16)
        hidden_parts = local_all_gather(local_all_gather(hidden, "local_chip"), "local_core")
        down_parts = jnp.swapaxes(
            down_matrix.reshape(chips, cores, hidden.shape[1], down_matrix.shape[1]), 0, 1
        )
        expert_out = jnp.einsum(
            "cyrh,cyhd->rd", hidden_parts, down_parts, preferred_element_type=jnp.float32
        )
        expert_out = expert_out.astype(jnp.bfloat16).reshape(
            inner_size, outer_size, slot_count, down_matrix.shape[1]
        )
        returned_rows = lax.all_to_all(expert_out, outer, 1, 1, tiled=True)
        returned_rows = lax.all_to_all(returned_rows, inner, 0, 0, tiled=True)
        flat_back = returned_rows.reshape(slots_all, returned_rows.shape[-1])
        back_position = (
            (route_ids % inner_size) * (outer_size * capacity) + (route_ids // inner_size) * capacity + route_slots
        )
        weights_kept = jnp.where(is_kept, route_weights, jnp.zeros((), jnp.float32))
        combine = jnp.zeros((tok_rows, slots_all), jnp.float32)
        for route in range(top_count):
            combine = combine + jnp.where(
                back_position[:, route : route + 1] == slot_index[None, :], weights_kept[:, route : route + 1], 0.0
            )
        mixed = jnp.dot(
            combine,
            flat_back.astype(jnp.float32),
            precision=lax.Precision.HIGHEST,
            preferred_element_type=jnp.float32,
        )
        return mixed.astype(jnp.bfloat16)

    return body


def solution(mesh):
    outer_size = mesh.devices.shape[0] // 4 if mesh.devices.shape[0] % 4 == 0 else mesh.devices.shape[0]
    inner_size = mesh.devices.shape[0] // outer_size
    local_size = mesh.devices.shape[1]
    core_size = 2 if local_size % 2 == 0 else 1
    split = Mesh(
        mesh.devices.reshape(outer_size, inner_size, local_size // core_size, core_size),
        ("node_outer", "node_inner", "local_chip", "local_core"),
    )
    node = ("node_outer", "node_inner")
    local = ("local_chip", "local_core")
    in_specs = (
        P(node, local),
        P(node, None),
        P(node, None),
        P(node, None),
        P(node, None),
        P(node, None, local),
        P(node, None, local),
        P(node, None, local),
    )
    out_specs = P(node, local)
    return jax.shard_map(
        make_body("node_outer", "node_inner"),
        mesh=split,
        in_specs=in_specs,
        out_specs=out_specs,
        check_vma=False,
    )
```

```python
import jax
import jax.numpy as jnp
from jax import lax
from jax.sharding import Mesh
from jax.sharding import PartitionSpec as P


def node_all_to_all(x, outer, inner):
    inner_size = lax.axis_size(inner)
    y = x.reshape(x.shape[0] // inner_size, inner_size, *x.shape[1:])
    y = lax.all_to_all(y, inner, 1, 1, tiled=True)
    y = lax.all_to_all(y, outer, 0, 0, tiled=True)
    return y.reshape(x.shape)


def local_all_gather(x, axis_name):
    count = lax.axis_size(axis_name)
    copies = jnp.broadcast_to(x[None], (count,) + x.shape)
    return lax.all_to_all(copies, axis_name, 0, 0, tiled=True)


def make_body(outer, inner):
    node = (outer, inner)

    def body(
        tokens, route_ids, route_slots, keep_mask, route_weights, gate_weight, up_weight, down_weight
    ):
        groups = lax.axis_size(node)
        tok_rows = tokens.shape[0]
        top_count = route_ids.shape[1]
        capacity = (5 * tok_rows * top_count + 4 * groups - 1) // (4 * groups)
        slots_all = groups * capacity
        is_kept = keep_mask > 0
        position = route_ids * capacity + route_slots
        target = jnp.where(is_kept, position, slots_all)
        slot_index = jnp.arange(slots_all, dtype=jnp.int32)
        dispatch = jnp.zeros((slots_all, tok_rows), jnp.bfloat16)
        for route in range(top_count):
            dispatch = dispatch + (slot_index[:, None] == target[None, :, route]).astype(jnp.bfloat16)
        gate_matrix = gate_weight[0]
        up_matrix = up_weight[0]
        down_matrix = down_weight[0]
        outgoing = jnp.dot(dispatch, tokens, preferred_element_type=jnp.float32).astype(tokens.dtype)
        outgoing = outgoing.reshape(groups, capacity, tokens.shape[1])
        outer_size = lax.axis_size(outer)
        inner_size = lax.axis_size(inner)
        chips = lax.axis_size("local_chip")
        cores = lax.axis_size("local_core")
        feature = tokens.shape[1]
        by_outer = outgoing.reshape(outer_size, inner_size, capacity, feature)
        by_outer = lax.all_to_all(by_outer, outer, 0, 0, tiled=True)
        copies = jnp.broadcast_to(
            jnp.swapaxes(by_outer, 0, 1)[:, None],
            (inner_size, chips, outer_size, capacity, feature),
        ).reshape(inner_size * chips, outer_size, capacity, feature)
        chip_rows = lax.all_to_all(copies, (inner, "local_chip"), 0, 0, tiled=True)
        chip_rows = chip_rows.reshape(inner_size, chips, outer_size, capacity, feature)
        core_index = lax.axis_index("local_core")
        sibling = (core_index + 1) % cores
        core_ring = [(i, (i + 1) % cores) for i in range(cores)]
        sibling_rows = lax.ppermute(chip_rows, "local_core", core_ring)
        slot_count = capacity

        def by_part(matrix):
            return jnp.swapaxes(matrix.reshape(chips, cores, feature, matrix.shape[1]), 0, 1)

        both_parts = by_part(jnp.concatenate([gate_matrix, up_matrix], axis=1))
        both_value = jnp.einsum(
            "xyzsd,ydh->xzsh",
            chip_rows,
            lax.dynamic_index_in_dim(both_parts, core_index, 0, keepdims=False),
            preferred_element_type=jnp.float32,
        ) + jnp.einsum(
            "xyzsd,ydh->xzsh",
            sibling_rows,
            lax.dynamic_index_in_dim(both_parts, sibling, 0, keepdims=False),
            preferred_element_type=jnp.float32,
        )
        both_value = both_value.reshape(groups * slot_count, 2 * gate_matrix.shape[1])
        gate_value = both_value[:, : gate_matrix.shape[1]]
        up_value = both_value[:, gate_matrix.shape[1] :]
        hidden = (jax.nn.silu(gate_value) * up_value).astype(jnp.bfloat16)
        hidden_chip = local_all_gather(hidden, "local_chip")
        hidden_sibling = lax.ppermute(hidden_chip, "local_core", core_ring)
        down_parts = jnp.swapaxes(
            down_matrix.reshape(chips, cores, hidden.shape[1], down_matrix.shape[1]), 0, 1
        )
        expert_out = jnp.einsum(
            "yrh,yhd->rd",
            hidden_chip,
            lax.dynamic_index_in_dim(down_parts, core_index, 0, keepdims=False),
            preferred_element_type=jnp.float32,
        ) + jnp.einsum(
            "yrh,yhd->rd",
            hidden_sibling,
            lax.dynamic_index_in_dim(down_parts, sibling, 0, keepdims=False),
            preferred_element_type=jnp.float32,
        )
        expert_out = expert_out.astype(jnp.bfloat16).reshape(
            inner_size, outer_size, slot_count, down_matrix.shape[1]
        )
        returned_rows = lax.all_to_all(expert_out, outer, 1, 1, tiled=True)
        returned_rows = lax.all_to_all(returned_rows, inner, 0, 0, tiled=True)
        flat_back = returned_rows.reshape(slots_all, returned_rows.shape[-1])
        back_position = (
            (route_ids % inner_size) * (outer_size * capacity) + (route_ids // inner_size) * capacity + route_slots
        )
        weights_kept = jnp.where(is_kept, route_weights, jnp.zeros((), jnp.float32))
        combine = jnp.zeros((tok_rows, slots_all), jnp.float32)
        for route in range(top_count):
            combine = combine + jnp.where(
                back_position[:, route : route + 1] == slot_index[None, :], weights_kept[:, route : route + 1], 0.0
            )
        mixed = jnp.dot(
            combine,
            flat_back.astype(jnp.float32),
            precision=lax.Precision.HIGHEST,
            preferred_element_type=jnp.float32,
        )
        return mixed.astype(jnp.bfloat16)

    return body


def solution(mesh):
    outer_size = mesh.devices.shape[0] // 4 if mesh.devices.shape[0] % 4 == 0 else mesh.devices.shape[0]
    inner_size = mesh.devices.shape[0] // outer_size
    local_size = mesh.devices.shape[1]
    core_size = 2 if local_size % 2 == 0 else 1
    split = Mesh(
        mesh.devices.reshape(outer_size, inner_size, local_size // core_size, core_size),
        ("node_outer", "node_inner", "local_chip", "local_core"),
    )
    node = ("node_outer", "node_inner")
    local = ("local_chip", "local_core")
    in_specs = (
        P(node, local),
        P(node, None),
        P(node, None),
        P(node, None),
        P(node, None),
        P(node, None, local),
        P(node, None, local),
        P(node, None, local),
    )
    out_specs = P(node, local)
    return jax.shard_map(
        make_body("node_outer", "node_inner"),
        mesh=split,
        in_specs=in_specs,
        out_specs=out_specs,
        check_vma=False,
    )
```

```python
import jax
import jax.numpy as jnp
from jax import lax
from jax.sharding import Mesh
from jax.sharding import PartitionSpec as P


def node_all_to_all(x, outer, inner):
    inner_size = lax.axis_size(inner)
    y = x.reshape(x.shape[0] // inner_size, inner_size, *x.shape[1:])
    y = lax.all_to_all(y, inner, 1, 1, tiled=True)
    y = lax.all_to_all(y, outer, 0, 0, tiled=True)
    return y.reshape(x.shape)


def local_all_gather(x, axis_name):
    count = lax.axis_size(axis_name)
    copies = jnp.broadcast_to(x[None], (count,) + x.shape)
    return lax.all_to_all(copies, axis_name, 0, 0, tiled=True)


def make_body(outer, inner):
    node = (outer, inner)

    def body(
        tokens, route_ids, route_slots, keep_mask, route_weights, gate_weight, up_weight, down_weight
    ):
        groups = lax.axis_size(node)
        tok_rows = tokens.shape[0]
        top_count = route_ids.shape[1]
        capacity = (5 * tok_rows * top_count + 4 * groups - 1) // (4 * groups)
        slots_all = groups * capacity
        is_kept = keep_mask > 0
        position = route_ids * capacity + route_slots
        target = jnp.where(is_kept, position, slots_all)
        slot_index = jnp.arange(slots_all, dtype=jnp.int32)
        dispatch = jnp.zeros((slots_all, tok_rows), jnp.bfloat16)
        for route in range(top_count):
            dispatch = dispatch + (slot_index[:, None] == target[None, :, route]).astype(jnp.bfloat16)
        gate_matrix = gate_weight[0]
        up_matrix = up_weight[0]
        down_matrix = down_weight[0]
        outgoing = jnp.dot(dispatch, tokens, preferred_element_type=jnp.float32).astype(tokens.dtype)
        outgoing = outgoing.reshape(groups, capacity, tokens.shape[1])
        outer_size = lax.axis_size(outer)
        inner_size = lax.axis_size(inner)
        chips = lax.axis_size("local_chip")
        cores = lax.axis_size("local_core")
        feature = tokens.shape[1]
        by_outer = outgoing.reshape(outer_size, inner_size, capacity, feature)
        by_outer = lax.all_to_all(by_outer, outer, 0, 0, tiled=True)
        copies = jnp.broadcast_to(
            jnp.swapaxes(by_outer, 0, 1)[:, None],
            (inner_size, chips, outer_size, capacity, feature),
        ).reshape(inner_size * chips, outer_size, capacity, feature)
        chip_rows = lax.all_to_all(copies, (inner, "local_chip"), 0, 0, tiled=True)
        chip_rows = chip_rows.reshape(inner_size, chips, outer_size, capacity, feature)
        row_parts = local_all_gather(chip_rows, "local_core")
        slot_count = capacity

        def by_part(matrix):
            return jnp.swapaxes(matrix.reshape(chips, cores, feature, matrix.shape[1]), 0, 1)

        both_value = jnp.einsum(
            "cxyzsd,cydh->xzsh",
            row_parts,
            by_part(jnp.concatenate([gate_matrix, up_matrix], axis=1)),
            preferred_element_type=jnp.float32,
        ).reshape(groups * slot_count, 2 * gate_matrix.shape[1])
        gate_value = both_value[:, : gate_matrix.shape[1]]
        up_value = both_value[:, gate_matrix.shape[1] :]
        hidden = (jax.nn.silu(gate_value) * up_value).astype(jnp.bfloat16)
        hidden_parts = local_all_gather(local_all_gather(hidden, "local_chip"), "local_core")
        down_parts = jnp.swapaxes(
            down_matrix.reshape(chips, cores, hidden.shape[1], down_matrix.shape[1]), 0, 1
        )
        expert_out = jnp.einsum(
            "cyrh,cyhd->rd", hidden_parts, down_parts, preferred_element_type=jnp.float32
        )
        expert_out = expert_out.astype(jnp.bfloat16).reshape(
            inner_size, outer_size, slot_count, down_matrix.shape[1]
        )
        returned_rows = lax.all_to_all(expert_out, inner, 0, 0, tiled=True)
        returned_rows = lax.all_to_all(returned_rows, outer, 1, 1, tiled=True)
        flat_back = returned_rows.reshape(slots_all, returned_rows.shape[-1])
        back_position = (
            (route_ids % inner_size) * (outer_size * capacity) + (route_ids // inner_size) * capacity + route_slots
        )
        weights_kept = jnp.where(is_kept, route_weights, jnp.zeros((), jnp.float32))
        combine = jnp.zeros((tok_rows, slots_all), jnp.float32)
        for route in range(top_count):
            combine = combine + jnp.where(
                back_position[:, route : route + 1] == slot_index[None, :], weights_kept[:, route : route + 1], 0.0
            )
        mixed = jnp.dot(
            combine,
            flat_back.astype(jnp.float32),
            precision=lax.Precision.HIGHEST,
            preferred_element_type=jnp.float32,
        )
        return mixed.astype(jnp.bfloat16)

    return body


def solution(mesh):
    outer_size = mesh.devices.shape[0] // 4 if mesh.devices.shape[0] % 4 == 0 else mesh.devices.shape[0]
    inner_size = mesh.devices.shape[0] // outer_size
    local_size = mesh.devices.shape[1]
    core_size = 2 if local_size % 2 == 0 else 1
    split = Mesh(
        mesh.devices.reshape(outer_size, inner_size, local_size // core_size, core_size),
        ("node_outer", "node_inner", "local_chip", "local_core"),
    )
    node = ("node_outer", "node_inner")
    local = ("local_chip", "local_core")
    in_specs = (
        P(node, local),
        P(node, None),
        P(node, None),
        P(node, None),
        P(node, None),
        P(node, None, local),
        P(node, None, local),
        P(node, None, local),
    )
    out_specs = P(node, local)
    return jax.shard_map(
        make_body("node_outer", "node_inner"),
        mesh=split,
        in_specs=in_specs,
        out_specs=out_specs,
        check_vma=False,
    )
```

```python
import jax
import jax.numpy as jnp
from jax import lax
from jax.sharding import Mesh
from jax.sharding import PartitionSpec as P


def node_all_to_all(x, outer, inner):
    inner_size = lax.axis_size(inner)
    y = x.reshape(x.shape[0] // inner_size, inner_size, *x.shape[1:])
    y = lax.all_to_all(y, inner, 1, 1, tiled=True)
    y = lax.all_to_all(y, outer, 0, 0, tiled=True)
    return y.reshape(x.shape)


def local_all_gather(x, axis_name):
    count = lax.axis_size(axis_name)
    copies = jnp.broadcast_to(x[None], (count,) + x.shape)
    return lax.all_to_all(copies, axis_name, 0, 0, tiled=True)


def make_body(outer, inner):
    node = (outer, inner)

    def body(
        tokens, route_ids, route_slots, keep_mask, route_weights, gate_weight, up_weight, down_weight
    ):
        groups = lax.axis_size(node)
        tok_rows = tokens.shape[0]
        top_count = route_ids.shape[1]
        capacity = (5 * tok_rows * top_count + 4 * groups - 1) // (4 * groups)
        slots_all = groups * capacity
        is_kept = keep_mask > 0
        position = route_ids * capacity + route_slots
        target = jnp.where(is_kept, position, slots_all)
        slot_index = jnp.arange(slots_all, dtype=jnp.int32)
        dispatch = jnp.zeros((slots_all, tok_rows), jnp.bfloat16)
        for route in range(top_count):
            dispatch = dispatch + (slot_index[:, None] == target[None, :, route]).astype(jnp.bfloat16)
        gate_matrix = gate_weight[0]
        up_matrix = up_weight[0]
        down_matrix = down_weight[0]
        outgoing = jnp.dot(dispatch, tokens, preferred_element_type=jnp.float32).astype(tokens.dtype)
        outgoing = outgoing.reshape(groups, capacity, tokens.shape[1])
        outer_size = lax.axis_size(outer)
        inner_size = lax.axis_size(inner)
        chips = lax.axis_size("local_chip")
        cores = lax.axis_size("local_core")
        feature = tokens.shape[1]
        by_outer = outgoing.reshape(outer_size, inner_size, capacity, feature)
        by_outer = lax.all_to_all(by_outer, outer, 0, 0, tiled=True)
        copies = jnp.broadcast_to(
            jnp.swapaxes(by_outer, 0, 1)[:, None],
            (inner_size, chips, outer_size, capacity, feature),
        ).reshape(inner_size * chips, outer_size, capacity, feature)
        chip_rows = lax.all_to_all(copies, (inner, "local_chip"), 0, 0, tiled=True)
        chip_rows = chip_rows.reshape(inner_size, chips, outer_size, capacity, feature)
        row_parts = local_all_gather(chip_rows, "local_core")
        slot_count = capacity

        def by_part(matrix):
            return jnp.swapaxes(matrix.reshape(chips, cores, feature, matrix.shape[1]), 0, 1)

        both_value = jnp.einsum(
            "cxyzsd,cydh->xzsh",
            row_parts,
            by_part(jnp.concatenate([gate_matrix, up_matrix], axis=1)),
            preferred_element_type=jnp.float32,
        ).reshape(groups * slot_count, 2 * gate_matrix.shape[1])
        gate_value = both_value[:, : gate_matrix.shape[1]]
        up_value = both_value[:, gate_matrix.shape[1] :]
        hidden = (jax.nn.silu(gate_value) * up_value).astype(jnp.bfloat16)
        core_index = lax.axis_index("local_core")
        sibling = (core_index + 1) % cores
        hidden_chip = local_all_gather(hidden, "local_chip")
        hidden_sibling = lax.ppermute(hidden_chip, "local_core", [(i, (i + 1) % cores) for i in range(cores)])
        down_parts = jnp.swapaxes(
            down_matrix.reshape(chips, cores, hidden.shape[1], down_matrix.shape[1]), 0, 1
        )
        expert_out = jnp.einsum(
            "yrh,yhd->rd",
            hidden_chip,
            lax.dynamic_index_in_dim(down_parts, core_index, 0, keepdims=False),
            preferred_element_type=jnp.float32,
        ) + jnp.einsum(
            "yrh,yhd->rd",
            hidden_sibling,
            lax.dynamic_index_in_dim(down_parts, sibling, 0, keepdims=False),
            preferred_element_type=jnp.float32,
        )
        expert_out = expert_out.astype(jnp.bfloat16).reshape(
            inner_size, outer_size, slot_count, down_matrix.shape[1]
        )
        returned_rows = lax.all_to_all(expert_out, inner, 0, 0, tiled=True)
        returned_rows = lax.all_to_all(returned_rows, outer, 1, 1, tiled=True)
        flat_back = returned_rows.reshape(slots_all, returned_rows.shape[-1])
        back_position = (
            (route_ids % inner_size) * (outer_size * capacity) + (route_ids // inner_size) * capacity + route_slots
        )
        weights_kept = jnp.where(is_kept, route_weights, jnp.zeros((), jnp.float32))
        combine = jnp.zeros((tok_rows, slots_all), jnp.float32)
        for route in range(top_count):
            combine = combine + jnp.where(
                back_position[:, route : route + 1] == slot_index[None, :], weights_kept[:, route : route + 1], 0.0
            )
        mixed = jnp.dot(
            combine,
            flat_back.astype(jnp.float32),
            precision=lax.Precision.HIGHEST,
            preferred_element_type=jnp.float32,
        )
        return mixed.astype(jnp.bfloat16)

    return body


def solution(mesh):
    outer_size = mesh.devices.shape[0] // 4 if mesh.devices.shape[0] % 4 == 0 else mesh.devices.shape[0]
    inner_size = mesh.devices.shape[0] // outer_size
    local_size = mesh.devices.shape[1]
    core_size = 2 if local_size % 2 == 0 else 1
    split = Mesh(
        mesh.devices.reshape(outer_size, inner_size, local_size // core_size, core_size),
        ("node_outer", "node_inner", "local_chip", "local_core"),
    )
    node = ("node_outer", "node_inner")
    local = ("local_chip", "local_core")
    in_specs = (
        P(node, local),
        P(node, None),
        P(node, None),
        P(node, None),
        P(node, None),
        P(node, None, local),
        P(node, None, local),
        P(node, None, local),
    )
    out_specs = P(node, local)
    return jax.shard_map(
        make_body("node_outer", "node_inner"),
        mesh=split,
        in_specs=in_specs,
        out_specs=out_specs,
        check_vma=False,
    )
```
